768 devices in a mesh: island: 96 (over x, z, core), fsdp: 8 (over y).
Axes of the slice: x: 4, y: 8, z: 12, core: 2. Of those that a mesh axis runs over, the one named last changes fastest.
Arguments:
- pseudo_grad: bfloat16 [96, 8192, 512], P('island', 'fsdp'), may hold values from -40 to 40
- error_buf: bfloat16 [96, 8192, 512], P('island', 'fsdp'), may hold values from -2 to 2
- params: bfloat16 [8192, 512], P('fsdp'), may hold values from -6 to 6
- momentum: float32 [96, 1024], P('island', 'fsdp'), may hold values from -4 to 4
- sel_blocks: int32 [96, 512], P('island', 'fsdp'), may hold values from 0 to 127, as said below
- coef_index: int32 [1024, 64], P('fsdp'), may hold values from 0 to 4095, as said below
- owner_map: int32 [1024], P('fsdp'), may hold values from 0 to 95, as said below
Outputs:
- new_params: bfloat16 [8192, 512], P('fsdp')
- new_error: bfloat16 [96, 8192, 512], P('island', 'fsdp')
- new_momentum: float32 [96, 1024], P('island', 'fsdp')
The draws below stay inside these ranges and needn't reach their ends.
Inputs may be any that keep to these rules, and one draw needn't show every extreme that they name: `sel_blocks`: each island's 64 entries for one shard are distinct blocks of that shard. `coef_index`: each row holds 64 distinct positions. `owner_map`: within each shard of 128 blocks an island owns at most 2 blocks, and some island owns exactly 2.
All inputs are finite; a program needn't handle non-finite values.
Results may differ from the reference program's by a relative error of at most 0.0032.
Values may be sent and summed in bfloat16 or wider, within the bound.
No kernel may reach another device: no remote copies, remote signals or barrier semaphores. Data moves between devices by JAX's collectives and lax.ppermute only.
A program may use at most 64 MiB of HBM per device.

```python
import jax
import jax.numpy as jnp
from jax import lax

D = 8192
KV_HEADS = 4
HEAD_DIM = 128
COEFS = 64
KVW = 512
BLK_DEV = 128
SEL = 64
OWN_CAP = 2
N_ISLAND = 96
N_FSDP = 8


def rising_factor(shard_pos):
    return 3.0 ** (shard_pos.astype(jnp.float32) / max(N_FSDP - 1, 1))


def draw_pseudo_grad(key, part):
    columns = KV_HEADS * HEAD_DIM
    subkeys = jax.random.split(jax.random.fold_in(key, 11), 5)
    row_scale = 10.0 ** jax.random.uniform(subkeys[0], (N_ISLAND, D, 1))
    col_scale = 10.0 ** jax.random.uniform(subkeys[1], (N_ISLAND, 1, columns))
    shard_pos = jnp.arange(D) // (D // N_FSDP)
    rising = rising_factor(shard_pos)[None, :, None]
    values_base = jax.random.normal(subkeys[4], (N_ISLAND, D, columns))
    return jnp.clip(values_base * row_scale * col_scale * rising / 6.0, -40.0, 40.0).astype(jnp.bfloat16)


def draw_momentum(key, part):
    per_shard = OWN_CAP * COEFS
    subkeys = jax.random.split(jax.random.fold_in(key, 23), 2)
    shard_pos = jnp.arange(N_FSDP * per_shard) // per_shard
    rising = rising_factor(shard_pos)[None, :]
    values_base = jax.random.normal(subkeys[1], (N_ISLAND, N_FSDP * per_shard))
    return jnp.clip(0.5 * values_base * rising, -4.0, 4.0)


def draw_sel_blocks(key, part):
    held_keys = jax.random.split(jax.random.fold_in(key, 53), 2)
    held_shard = jax.random.randint(held_keys[0], (), 0, N_FSDP).astype(jnp.int32)
    held_block = jax.random.randint(held_keys[1], (), 0, BLK_DEV).astype(jnp.int32)
    subkeys = jax.random.split(jax.random.fold_in(key, 31), N_ISLAND * N_FSDP)
    shard_pos = (jnp.arange(N_ISLAND * N_FSDP) % N_FSDP).astype(jnp.int32)

    def one_list(single, shard_here):
        full_list = jax.random.permutation(single, BLK_DEV)[:SEL].astype(jnp.int32)
        short_list = jax.random.permutation(single, BLK_DEV - 1)[:SEL].astype(jnp.int32)
        short_list = short_list + (short_list >= held_block).astype(jnp.int32)
        return jnp.where(shard_here == held_shard, short_list, full_list)
    picks = jax.vmap(one_list)(subkeys, shard_pos)
    return picks.reshape(N_ISLAND, N_FSDP * SEL).astype(jnp.int32)


def draw_coef_index(key, part):
    subkeys = jax.random.split(jax.random.fold_in(key, 37), N_FSDP * BLK_DEV)
    picks = jax.vmap(lambda single: jax.random.permutation(single, 4096)[:COEFS])(subkeys)
    return picks.astype(jnp.int32)


def owners_of_shard(single):
    first_key, second_key = jax.random.split(single)
    slot_total = N_ISLAND * OWN_CAP
    shuffled = jax.random.permutation(first_key, slot_total)
    leading = shuffled[0] // OWN_CAP
    slot_ids = jnp.arange(slot_total)
    position = jnp.argsort(shuffled)
    scores = jnp.where(slot_ids // OWN_CAP == leading, slot_ids - slot_total, position)
    ordering = jnp.argsort(scores)
    owners = ordering[:BLK_DEV] // OWN_CAP
    mixing = jax.random.permutation(second_key, BLK_DEV)
    return owners[mixing]


def draw_owner_map(key, part):
    subkeys = jax.random.split(jax.random.fold_in(key, 41), N_FSDP)
    return jax.vmap(owners_of_shard)(subkeys).reshape(N_FSDP * BLK_DEV).astype(jnp.int32)


def levels(key, extent, pieces, smallest, high):
    factor_of, own = 1.0, jax.random.fold_in(key, 6)
    for dim, shards_of in pieces:
        heights = jnp.exp(jax.random.uniform(jax.random.fold_in(own, dim), (shards_of,), jnp.float32, smallest / len(pieces), high / len(pieces)))
        factor_of = factor_of * jnp.repeat(heights, extent[dim] // shards_of).reshape([-1 if axis == dim else 1 for axis in range(len(extent))])
    return factor_of


def noise(stream_key, extent, scale, bound, cuts=(), kind=jnp.bfloat16):
    entries = scale * jax.random.normal(stream_key, extent, jnp.float32)
    if cuts:
        entries = entries * levels(stream_key, extent, cuts, -0.22, 0.18)
    return jnp.clip(entries, -bound, bound).astype(kind)


def setup_inputs(seed: int = 0) -> dict:
    key_of = jax.random.split(jax.random.key(seed), 8)
    return {
        "pseudo_grad": draw_pseudo_grad(jax.random.fold_in(key_of[7], 71), 0),
        "error_buf": noise(key_of[1], (N_ISLAND, D, KVW), 0.3, 2.0, ((0, 96), (1, 8))),
        "params": noise(key_of[2], (D, KVW), 1.0, 6.0, ((0, 8),)),
        "momentum": draw_momentum(jax.random.fold_in(key_of[7], 71), 0),
        "sel_blocks": draw_sel_blocks(jax.random.fold_in(key_of[7], 71), 0),
        "coef_index": draw_coef_index(jax.random.fold_in(key_of[7], 71), 0),
        "owner_map": draw_owner_map(jax.random.fold_in(key_of[7], 71), 0),
    }


BETA_FACTOR = 0.9
OUTER_RATE = 0.5
EPSILON = 1e-06
precise_mode = lax.Precision.HIGHEST

def cosine_table():
    freqs = jnp.arange(64, dtype=jnp.float32)[:, None]
    points = jnp.arange(64, dtype=jnp.float32)[None, :]
    scaling = jnp.where(freqs == 0.0, jnp.sqrt(1.0 / 64.0), jnp.sqrt(2.0 / 64.0))
    return scaling * jnp.cos(jnp.pi * (2.0 * points + 1.0) * freqs / 128.0)

def to_blocks(field):
    row_blocks = field.shape[0] // 64
    col_blocks = field.shape[1] // 64
    return field.reshape(row_blocks, 64, col_blocks, 64).transpose(0, 2, 1, 3).reshape(row_blocks * col_blocks, 64, 64)

def from_blocks(blocks, row_total, col_total):
    row_blocks = row_total // 64
    col_blocks = col_total // 64
    return blocks.reshape(row_blocks, col_blocks, 64, 64).transpose(0, 2, 1, 3).reshape(row_total, col_total)

def forward_blocks(cosine, blocks):
    return jnp.einsum('ij,bjk,lk->bil', cosine, blocks, cosine, precision=precise_mode)

def inverse_blocks(cosine, blocks):
    return jnp.einsum('ji,bjk,kl->bil', cosine, blocks, cosine, precision=precise_mode)

def scatter_coefs(values, positions):
    amount = values.shape[0]
    return jnp.zeros((amount, 4096), jnp.float32).at[jnp.arange(amount)[:, None], positions].set(values)

def reference(pseudo_grad, error_buf, params, momentum, sel_blocks, coef_index, owner_map):
    cosine = cosine_table()
    n_blocks = coef_index.shape[0]
    shard_blocks = n_blocks // N_FSDP
    shard_picks = sel_blocks.shape[1] // N_FSDP
    coef_count = coef_index.shape[1]
    block_ids = jnp.arange(n_blocks, dtype=jnp.int32)
    shard_of = block_ids // shard_blocks
    offsets = (jnp.arange(N_FSDP, dtype=jnp.int32) * shard_blocks)[:, None]

    def island_step(inputs):
        grad_part, error_part, chosen = inputs
        summed = grad_part.astype(jnp.float32) + error_part.astype(jnp.float32)
        blocks = to_blocks(summed)
        spectra = forward_blocks(cosine, blocks).reshape(n_blocks, 4096)
        picked = jnp.take_along_axis(spectra, coef_index, axis=1)
        global_ids = (chosen.reshape(N_FSDP, shard_picks) + offsets).reshape(-1)
        chosen_mask = jnp.zeros((n_blocks,), jnp.float32).at[global_ids].set(1.0)
        outgoing = picked * chosen_mask[:, None]
        rebuilt = inverse_blocks(cosine, scatter_coefs(outgoing, coef_index).reshape(n_blocks, 64, 64))
        fresh_error = from_blocks(blocks - rebuilt, summed.shape[0], summed.shape[1]).astype(jnp.bfloat16)
        return (fresh_error, outgoing, chosen_mask)
    new_error, outgoing_all, masks_all = lax.map(island_step, (pseudo_grad, error_buf, sel_blocks))
    totals = lax.optimization_barrier(jnp.sum(outgoing_all, axis=0))
    counts = lax.optimization_barrier(jnp.sum(masks_all, axis=0))
    average = totals / jnp.maximum(counts, 1.0)[:, None]
    earlier = (owner_map[None, :] == owner_map[:, None]) & (shard_of[None, :] == shard_of[:, None]) & (block_ids[None, :] < block_ids[:, None])
    slot_of = lax.optimization_barrier(jnp.sum(earlier.astype(jnp.int32), axis=1))
    capacity = momentum.shape[1] // (N_FSDP * coef_count)
    grouped = momentum.reshape(N_ISLAND, N_FSDP, capacity, coef_count)
    previous = grouped[owner_map, shard_of, slot_of]
    refreshed = BETA_FACTOR * previous + average
    new_grouped = (BETA_FACTOR * grouped).at[owner_map, shard_of, slot_of].set(refreshed)
    update_coef = average + BETA_FACTOR * refreshed
    update = inverse_blocks(cosine, scatter_coefs(update_coef, coef_index).reshape(n_blocks, 64, 64)).astype(jnp.bfloat16)
    update = lax.optimization_barrier(update).astype(jnp.float32)
    total_square = jnp.sum(update * update)
    scale_root = jnp.sqrt(total_square / (D * KVW) + EPSILON)
    shifted = from_blocks(update, D, KVW)
    new_params = (params.astype(jnp.float32) - OUTER_RATE * shifted / scale_root).astype(jnp.bfloat16)
    return (new_params, new_error, new_grouped.reshape(N_ISLAND, N_FSDP * capacity * coef_count))
```

```python
import functools

import jax
import jax.numpy as jnp
from jax import lax
from jax.sharding import PartitionSpec as P

BETA_FACTOR = 0.9
OUTER_RATE = 0.5
EPSILON = 1e-06
precise_mode = lax.Precision.HIGHEST


def cosine_table():
    freqs = jnp.arange(64, dtype=jnp.float32)[:, None]
    points = jnp.arange(64, dtype=jnp.float32)[None, :]
    scaling = jnp.where(freqs == 0.0, jnp.sqrt(1.0 / 64.0), jnp.sqrt(2.0 / 64.0))
    return scaling * jnp.cos(jnp.pi * (2.0 * points + 1.0) * freqs / 128.0)


def to_blocks(field):
    row_blocks = field.shape[0] // 64
    col_blocks = field.shape[1] // 64
    return (
        field.reshape(row_blocks, 64, col_blocks, 64)
        .transpose(0, 2, 1, 3)
        .reshape(row_blocks * col_blocks, 64, 64)
    )


def from_blocks(blocks, row_total, col_total):
    row_blocks = row_total // 64
    col_blocks = col_total // 64
    return (
        blocks.reshape(row_blocks, col_blocks, 64, 64)
        .transpose(0, 2, 1, 3)
        .reshape(row_total, col_total)
    )


def one_hot_rows(table, index):
    hot = (index[..., None] == jnp.arange(table.shape[0], dtype=jnp.int32)).astype(jnp.float32)
    return jnp.einsum("...t,tc->...c", hot, table, precision=precise_mode)


def decode(row_cos, col_cos, values):
    return jnp.einsum("bkj,bkl->bjl", row_cos * values[:, :, None], col_cos, precision=precise_mode)


def butterfly_sum(value, axis, radices):
    size = lax.axis_size(axis)
    here = lax.axis_index(axis)
    stride = 1
    for radix in radices:
        digit = (here // stride) % radix
        pieces = {0: value}
        for shift in range(1, radix):
            perm = []
            for src in range(size):
                d = (src // stride) % radix
                perm.append((src, src + ((d + shift) % radix - d) * stride))
            pieces[shift] = lax.ppermute(value, axis, perm)
        if radix == 2:
            value = pieces[0] + pieces[1]
        else:
            ordered = []
            for e in range(radix):
                pick = pieces[0]
                for shift in range(1, radix):
                    pick = jnp.where((digit - shift) % radix == e, pieces[shift], pick)
                ordered.append(pick)
            value = ordered[0]
            for e in range(1, radix):
                value = value + ordered[e]
        stride *= radix
    return value


def radices_of(sub_sizes):
    out = []
    for part in reversed(sub_sizes):
        left = part
        for prime in (2, 3, 5, 7):
            while left % prime == 0:
                out.append(prime)
                left //= prime
        if left > 1:
            out.append(left)
    return out


def on_device(island_radices, fsdp_radices, pseudo_grad, error_buf, params, momentum, sel_blocks, coef_index, owner_map):
    cosine = cosine_table()
    my_island = lax.axis_index("island")
    shard_rows = params.shape[0]
    columns = params.shape[1]
    n_blocks = coef_index.shape[0]
    coef_total = coef_index.shape[1]
    capacity = momentum.shape[1] // coef_total

    summed = pseudo_grad[0].astype(jnp.float32) + error_buf[0].astype(jnp.float32)
    blocks = to_blocks(summed)
    row_cos = one_hot_rows(cosine, coef_index // 64)
    col_cos = one_hot_rows(cosine, coef_index % 64)
    half = jnp.einsum("bkj,bjl->bkl", row_cos, blocks, precision=precise_mode)
    picked = jnp.sum(half * col_cos, axis=2)

    chosen = sel_blocks[0]
    block_ids = jnp.arange(n_blocks, dtype=jnp.int32)
    chosen_mask = jnp.any(chosen[:, None] == block_ids[None, :], axis=0).astype(jnp.float32)
    outgoing = picked * chosen_mask[:, None]

    earlier = (owner_map[None, :] == owner_map[:, None]) & (block_ids[None, :] < block_ids[:, None])
    slot_of = jnp.sum(earlier.astype(jnp.int32), axis=1)
    target = owner_map * capacity + slot_of
    own_slots = my_island * capacity + jnp.arange(capacity, dtype=jnp.int32)
    owned_mask = (target[None, :] == own_slots[:, None]).astype(jnp.float32)
    mine = momentum[0].reshape(capacity, coef_total)
    held = jnp.einsum("sb,sk->bk", owned_mask, mine, precision=precise_mode)

    mask_rows = -(-n_blocks // coef_total)
    mask_part = jnp.pad(chosen_mask, (0, mask_rows * coef_total - n_blocks)).reshape(mask_rows, coef_total)
    payload = jnp.concatenate([outgoing, held, mask_part], axis=0)
    reduced = butterfly_sum(payload, "island", island_radices)
    totals = reduced[:n_blocks]
    previous = reduced[n_blocks : 2 * n_blocks]
    counts = reduced[2 * n_blocks :].reshape(-1)[:n_blocks]

    rebuilt = decode(row_cos, col_cos, outgoing)
    new_error = from_blocks(blocks - rebuilt, shard_rows, columns).astype(jnp.bfloat16)[None]

    average = totals / jnp.maximum(counts, 1.0)[:, None]
    refreshed = BETA_FACTOR * previous + average
    update_coef = average + BETA_FACTOR * refreshed

    owned_live = jnp.sum(owned_mask, axis=1) > 0.0
    owned_fresh = jnp.dot(owned_mask, refreshed, precision=precise_mode)
    kept = BETA_FACTOR * mine
    new_momentum = jnp.where(owned_live[:, None], owned_fresh, kept).reshape(1, capacity * coef_total)

    update = decode(row_cos, col_cos, update_coef).astype(jnp.bfloat16).astype(jnp.float32)
    local_square = jnp.sum(update * update)
    total_square = butterfly_sum(local_square, "fsdp", fsdp_radices)
    scale_root = jnp.sqrt(total_square / (shard_rows * lax.axis_size("fsdp") * columns) + EPSILON)
    shifted = from_blocks(update, shard_rows, columns)
    new_params = (params.astype(jnp.float32) - OUTER_RATE * shifted / scale_root).astype(
        jnp.bfloat16
    )
    return (new_params, new_error, new_momentum)


def solution(mesh):
    in_specs = (
        P("island", "fsdp", None),
        P("island", "fsdp", None),
        P("fsdp", None),
        P("island", "fsdp"),
        P("island", "fsdp"),
        P("fsdp", None),
        P("fsdp"),
    )
    out_specs = (P("fsdp", None), P("island", "fsdp", None), P("island", "fsdp"))
    island_radices = radices_of((4, 12, 2))
    if mesh.shape["island"] != 96:
        island_radices = radices_of((mesh.shape["island"],))
    fsdp_radices = radices_of((mesh.shape["fsdp"],))
    body = functools.partial(on_device, island_radices, fsdp_radices)
    return jax.shard_map(
        body, mesh=mesh, in_specs=in_specs, out_specs=out_specs, check_vma=False
    )
```

```python
import functools

import jax
import jax.numpy as jnp
from jax import lax
from jax.sharding import PartitionSpec as P

BETA_FACTOR = 0.9
OUTER_RATE = 0.5
EPSILON = 1e-06
precise_mode = lax.Precision.HIGHEST
ERR_CHUNKS = 4
UPD_CHUNKS = 2


def cosine_table():
    freqs = jnp.arange(64, dtype=jnp.float32)[:, None]
    points = jnp.arange(64, dtype=jnp.float32)[None, :]
    scaling = jnp.where(freqs == 0.0, jnp.sqrt(1.0 / 64.0), jnp.sqrt(2.0 / 64.0))
    return scaling * jnp.cos(jnp.pi * (2.0 * points + 1.0) * freqs / 128.0)


def to_blocks(field):
    row_blocks = field.shape[0] // 64
    col_blocks = field.shape[1] // 64
    return (
        field.reshape(row_blocks, 64, col_blocks, 64)
        .transpose(0, 2, 1, 3)
        .reshape(row_blocks * col_blocks, 64, 64)
    )


def from_blocks(blocks, row_total, col_total):
    row_blocks = row_total // 64
    col_blocks = col_total // 64
    return (
        blocks.reshape(row_blocks, col_blocks, 64, 64)
        .transpose(0, 2, 1, 3)
        .reshape(row_total, col_total)
    )


def one_hot_rows(table, index):
    hot = (index[..., None] == jnp.arange(table.shape[0], dtype=jnp.int32)).astype(jnp.float32)
    return jnp.einsum("...t,tc->...c", hot, table, precision=precise_mode)


def decode(row_cos, col_cos, values):
    return jnp.einsum("bkj,bkl->bjl", row_cos * values[:, :, None], col_cos, precision=precise_mode)


def butterfly_sum(value, axis, radices):
    size = lax.axis_size(axis)
    here = lax.axis_index(axis)
    stride = 1
    for radix in radices:
        digit = (here // stride) % radix
        pieces = {0: value}
        for shift in range(1, radix):
            perm = []
            for src in range(size):
                d = (src // stride) % radix
                perm.append((src, src + ((d + shift) % radix - d) * stride))
            pieces[shift] = lax.ppermute(value, axis, perm)
        if radix == 2:
            value = pieces[0] + pieces[1]
        else:
            ordered = []
            for e in range(radix):
                pick = pieces[0]
                for shift in range(1, radix):
                    pick = jnp.where((digit - shift) % radix == e, pieces[shift], pick)
                ordered.append(pick)
            value = ordered[0]
            for e in range(1, radix):
                value = value + ordered[e]
        stride *= radix
    return value


def radices_of(sub_sizes):
    out = []
    for part in reversed(sub_sizes):
        left = part
        for prime in (2, 3, 5, 7):
            while left % prime == 0:
                out.append(prime)
                left //= prime
        if left > 1:
            out.append(left)
    return out


def on_device(island_radices, fsdp_radices, *args):
    return step_body(island_radices, fsdp_radices, *args)


def step_body(island_radices, fsdp_radices, pseudo_grad, error_buf, params, momentum, sel_blocks, coef_index, owner_map):
    cosine = cosine_table()
    my_island = lax.axis_index("island")
    shard_rows = params.shape[0]
    columns = params.shape[1]
    n_blocks = coef_index.shape[0]
    coef_total = coef_index.shape[1]
    capacity = momentum.shape[1] // coef_total

    summed = pseudo_grad[0].astype(jnp.float32) + error_buf[0].astype(jnp.float32)
    blocks = to_blocks(summed)
    row_cos = one_hot_rows(cosine, coef_index // 64)
    col_cos = one_hot_rows(cosine, coef_index % 64)
    half = jnp.einsum("bkj,bjl->bkl", row_cos, blocks, precision=precise_mode)
    picked = jnp.sum(half * col_cos, axis=2)

    chosen = sel_blocks[0]
    block_ids = jnp.arange(n_blocks, dtype=jnp.int32)
    chosen_mask = jnp.any(chosen[:, None] == block_ids[None, :], axis=0).astype(jnp.float32)
    outgoing = picked * chosen_mask[:, None]

    earlier = (owner_map[None, :] == owner_map[:, None]) & (block_ids[None, :] < block_ids[:, None])
    slot_of = jnp.sum(earlier.astype(jnp.int32), axis=1)
    target = owner_map * capacity + slot_of
    own_slots = my_island * capacity + jnp.arange(capacity, dtype=jnp.int32)
    owned_mask = (target[None, :] == own_slots[:, None]).astype(jnp.float32)
    mine = momentum[0].reshape(capacity, coef_total)
    held = jnp.einsum("sb,sk->bk", owned_mask, mine, precision=precise_mode)

    mask_rows = -(-n_blocks // coef_total)
    mask_part = jnp.pad(chosen_mask, (0, mask_rows * coef_total - n_blocks)).reshape(mask_rows, coef_total)
    payload = jnp.concatenate([outgoing, held, mask_part], axis=0)
    reduced = butterfly_sum(payload, "island", island_radices)
    totals = reduced[:n_blocks]
    previous = reduced[n_blocks : 2 * n_blocks]
    counts = reduced[2 * n_blocks :].reshape(-1)[:n_blocks]

    row_blocks = shard_rows // 64
    err_chunks = ERR_CHUNKS if row_blocks % ERR_CHUNKS == 0 else 1
    per = n_blocks // err_chunks
    error_parts = []
    for c in range(err_chunks):
        part = slice(c * per, (c + 1) * per)
        rebuilt = decode(row_cos[part], col_cos[part], outgoing[part])
        fresh = from_blocks(blocks[part] - rebuilt, shard_rows // err_chunks, columns)
        error_parts.append(fresh.astype(jnp.bfloat16))
    new_error = jnp.concatenate(error_parts, axis=0)[None]

    average = totals / jnp.maximum(counts, 1.0)[:, None]
    refreshed = BETA_FACTOR * previous + average
    update_coef = average + BETA_FACTOR * refreshed

    owned_live = jnp.sum(owned_mask, axis=1) > 0.0
    owned_fresh = jnp.dot(owned_mask, refreshed, precision=precise_mode)
    kept = BETA_FACTOR * mine
    new_momentum = jnp.where(owned_live[:, None], owned_fresh, kept).reshape(1, capacity * coef_total)

    local_square = jnp.sum(update_coef * update_coef)
    total_square = butterfly_sum(local_square, "fsdp", fsdp_radices)
    scale_root = jnp.sqrt(total_square / (shard_rows * lax.axis_size("fsdp") * columns) + EPSILON)

    upd_chunks = UPD_CHUNKS if row_blocks % UPD_CHUNKS == 0 else 1
    per = n_blocks // upd_chunks
    update_parts = []
    for c in range(upd_chunks):
        part = slice(c * per, (c + 1) * per)
        update = decode(row_cos[part], col_cos[part], update_coef[part]).astype(jnp.bfloat16)
        update_parts.append(from_blocks(update, shard_rows // upd_chunks, columns))
    shifted = jnp.concatenate(update_parts, axis=0).astype(jnp.float32)
    new_params = (params.astype(jnp.float32) - OUTER_RATE * shifted / scale_root).astype(
        jnp.bfloat16
    )
    return (new_params, new_error, new_momentum)


def solution(mesh):
    in_specs = (
        P("island", "fsdp", None),
        P("island", "fsdp", None),
        P("fsdp", None),
        P("island", "fsdp"),
        P("island", "fsdp"),
        P("fsdp", None),
        P("fsdp"),
    )
    out_specs = (P("fsdp", None), P("island", "fsdp", None), P("island", "fsdp"))
    island_radices = radices_of((4, 12, 2))
    if mesh.shape["island"] != 96:
        island_radices = radices_of((mesh.shape["island"],))
    fsdp_radices = radices_of((mesh.shape["fsdp"],))
    body = functools.partial(on_device, island_radices, fsdp_radices)
    return jax.shard_map(
        body, mesh=mesh, in_specs=in_specs, out_specs=out_specs, check_vma=False
    )
```

```python
import functools

import jax
import jax.numpy as jnp
from jax import lax
from jax.sharding import PartitionSpec as P
from jax.experimental import pallas as pl
from jax.experimental.pallas import tpu as pltpu

BETA_FACTOR = 0.9
OUTER_RATE = 0.5
EPSILON = 1e-06
precise_mode = lax.Precision.HIGHEST


def cosine_table():
    freqs = jnp.arange(64, dtype=jnp.float32)[:, None]
    points = jnp.arange(64, dtype=jnp.float32)[None, :]
    scaling = jnp.where(freqs == 0.0, jnp.sqrt(1.0 / 64.0), jnp.sqrt(2.0 / 64.0))
    return scaling * jnp.cos(jnp.pi * (2.0 * points + 1.0) * freqs / 128.0)


def to_blocks(field):
    row_blocks = field.shape[0] // 64
    col_blocks = field.shape[1] // 64
    return (
        field.reshape(row_blocks, 64, col_blocks, 64)
        .transpose(0, 2, 1, 3)
        .reshape(row_blocks * col_blocks, 64, 64)
    )


def from_blocks(blocks, row_total, col_total):
    row_blocks = row_total // 64
    col_blocks = col_total // 64
    return (
        blocks.reshape(row_blocks, col_blocks, 64, 64)
        .transpose(0, 2, 1, 3)
        .reshape(row_total, col_total)
    )


def one_hot_rows(table, index):
    hot = (index[..., None] == jnp.arange(table.shape[0], dtype=jnp.int32)).astype(jnp.float32)
    return jnp.einsum("...t,tc->...c", hot, table, precision=precise_mode)


def decode(row_cos, col_cos, values):
    return jnp.einsum("bkj,bkl->bjl", row_cos * values[:, :, None], col_cos, precision=precise_mode)


def butterfly_sum(value, axis, radices, tag):
    size = lax.axis_size(axis)
    here = lax.axis_index(axis)
    stride = 1
    done_rounds = []
    for radix in radices:
        digit = (here // stride) % radix
        pieces = {0: value}
        for shift in range(1, radix):
            perm = []
            for src in range(size):
                d = (src // stride) % radix
                perm.append((src, src + ((d + shift) % radix - d) * stride))
            with jax.named_scope(f"{tag}{len(done_rounds)}s{shift}"):
                pieces[shift] = lax.ppermute(value, axis, perm)
        if radix == 2:
            value = pieces[0] + pieces[1]
        else:
            ordered = []
            for e in range(radix):
                pick = pieces[0]
                for shift in range(1, radix):
                    pick = jnp.where((digit - shift) % radix == e, pieces[shift], pick)
                ordered.append(pick)
            value = ordered[0]
            for e in range(1, radix):
                value = value + ordered[e]
        stride *= radix
        done_rounds.append(radix)
    return value


def radices_of(sub_sizes):
    out = []
    for part in reversed(sub_sizes):
        left = part
        for prime in (2, 3, 5, 7):
            while left % prime == 0:
                out.append(prime)
                left //= prime
        if left > 1:
            out.append(left)
    return out


def _rows(idx_col, cos):
    hot = (idx_col == lax.broadcasted_iota(jnp.int32, (idx_col.shape[0], 64), 1)).astype(jnp.float32)
    return jnp.dot(hot, cos, precision=precise_mode, preferred_element_type=jnp.float32)


def _encode_kernel(cos_ref, idx_ref, mask_ref, g_ref, e_ref, sent_ref, err_ref):
    cos = cos_ref[...]
    for cb in range(idx_ref.shape[2]):
        cols = slice(cb * 64, (cb + 1) * 64)
        idx = idx_ref[0, :, cb : cb + 1]
        row_cos = _rows(idx // 64, cos)
        col_cos = _rows(idx % 64, cos)
        x = g_ref[:, cols].astype(jnp.float32) + e_ref[:, cols].astype(jnp.float32)
        half = jnp.dot(row_cos, x, precision=precise_mode, preferred_element_type=jnp.float32)
        sent = jnp.sum(half * col_cos, axis=1, keepdims=True) * mask_ref[0, :, cb : cb + 1]
        sent_ref[0, :, cb : cb + 1] = sent
        rebuilt = jnp.dot((row_cos * sent).T, col_cos, precision=precise_mode, preferred_element_type=jnp.float32)
        err_ref[:, cols] = (x - rebuilt).astype(err_ref.dtype)


def encode(grad, error, idx_t3, mask3):
    rows, columns = grad.shape
    row_blocks = rows // 64
    col_blocks = columns // 64
    return pl.pallas_call(
        _encode_kernel,
        grid=(row_blocks,),
        in_specs=[
            pl.BlockSpec((64, 64), lambda i: (0, 0)),
            pl.BlockSpec((1, 64, col_blocks), lambda i: (i, 0, 0)),
            pl.BlockSpec((1, 1, col_blocks), lambda i: (i, 0, 0)),
            pl.BlockSpec((64, columns), lambda i: (i, 0)),
            pl.BlockSpec((64, columns), lambda i: (i, 0)),
        ],
        out_specs=[
            pl.BlockSpec((1, 64, col_blocks), lambda i: (i, 0, 0)),
            pl.BlockSpec((64, columns), lambda i: (i, 0)),
        ],
        out_shape=[
            jax.ShapeDtypeStruct((row_blocks, 64, col_blocks), jnp.float32),
            jax.ShapeDtypeStruct((rows, columns), jnp.bfloat16),
        ],
        compiler_params=pltpu.CompilerParams(dimension_semantics=("parallel",)),
    )(cosine_table(), idx_t3, mask3, grad, error)


def _apply_kernel(rate, cos_ref, idx_ref, coef_ref, scale_ref, p_ref, out_ref):
    cos = cos_ref[...]
    scale = scale_ref[0, 0]
    for cb in range(idx_ref.shape[2]):
        cols = slice(cb * 64, (cb + 1) * 64)
        idx = idx_ref[0, :, cb : cb + 1]
        row_cos = _rows(idx // 64, cos)
        col_cos = _rows(idx % 64, cos)
        coef = coef_ref[0, :, cb : cb + 1]
        update = jnp.dot((row_cos * coef).T, col_cos, precision=precise_mode, preferred_element_type=jnp.float32)
        update = update.astype(jnp.bfloat16).astype(jnp.float32)
        out_ref[:, cols] = (p_ref[:, cols].astype(jnp.float32) - rate * update / scale).astype(out_ref.dtype)


def apply_update(params, idx_t3, coef3, scale, rate):
    rows, columns = params.shape
    row_blocks = rows // 64
    col_blocks = columns // 64
    return pl.pallas_call(
        functools.partial(_apply_kernel, rate),
        grid=(row_blocks,),
        in_specs=[
            pl.BlockSpec((64, 64), lambda i: (0, 0)),
            pl.BlockSpec((1, 64, col_blocks), lambda i: (i, 0, 0)),
            pl.BlockSpec((1, 64, col_blocks), lambda i: (i, 0, 0)),
            pl.BlockSpec(memory_space=pltpu.SMEM),
            pl.BlockSpec((64, columns), lambda i: (i, 0)),
        ],
        out_specs=pl.BlockSpec((64, columns), lambda i: (i, 0)),
        out_shape=jax.ShapeDtypeStruct((rows, columns), jnp.bfloat16),
        compiler_params=pltpu.CompilerParams(dimension_semantics=("parallel",)),
    )(cosine_table(), idx_t3, coef3, scale.reshape(1, 1), params)


def on_device(island_radices, fsdp_radices, pseudo_grad, error_buf, params, momentum, sel_blocks, coef_index, owner_map):
    my_island = lax.axis_index("island")
    shard_rows = params.shape[0]
    columns = params.shape[1]
    n_blocks = coef_index.shape[0]
    coef_total = coef_index.shape[1]
    capacity = momentum.shape[1] // coef_total
    row_blocks = shard_rows // 64
    col_blocks = columns // 64

    chosen = sel_blocks[0]
    block_ids = jnp.arange(n_blocks, dtype=jnp.int32)
    chosen_mask = jnp.any(chosen[:, None] == block_ids[None, :], axis=0).astype(jnp.float32)
    idx_t3 = coef_index.reshape(row_blocks, col_blocks, coef_total).transpose(0, 2, 1)
    sent3, fresh_error = encode(pseudo_grad[0], error_buf[0], idx_t3, chosen_mask.reshape(row_blocks, 1, col_blocks))
    new_error = fresh_error[None]
    outgoing = sent3.transpose(0, 2, 1).reshape(n_blocks, coef_total)

    earlier = (owner_map[None, :] == owner_map[:, None]) & (block_ids[None, :] < block_ids[:, None])
    slot_of = jnp.sum(earlier.astype(jnp.int32), axis=1)
    target = owner_map * capacity + slot_of
    own_slots = my_island * capacity + jnp.arange(capacity, dtype=jnp.int32)
    owned_mask = (target[None, :] == own_slots[:, None]).astype(jnp.float32)
    mine = momentum[0].reshape(capacity, coef_total)
    held = jnp.einsum("sb,sk->bk", owned_mask, mine, precision=precise_mode)

    mask_rows = -(-n_blocks // coef_total)
    mask_part = jnp.pad(chosen_mask, (0, mask_rows * coef_total - n_blocks)).reshape(mask_rows, coef_total)
    payload = jnp.concatenate([outgoing, held, mask_part], axis=0)
    reduced = butterfly_sum(payload, "island", island_radices, "isl")
    totals = reduced[:n_blocks]
    previous = reduced[n_blocks : 2 * n_blocks]
    counts = reduced[2 * n_blocks :].reshape(-1)[:n_blocks]

    average = totals / jnp.maximum(counts, 1.0)[:, None]
    refreshed = BETA_FACTOR * previous + average
    update_coef = average + BETA_FACTOR * refreshed

    owned_live = jnp.sum(owned_mask, axis=1) > 0.0
    owned_fresh = jnp.dot(owned_mask, refreshed, precision=precise_mode)
    kept = BETA_FACTOR * mine
    new_momentum = jnp.where(owned_live[:, None], owned_fresh, kept).reshape(1, capacity * coef_total)

    local_square = jnp.sum(update_coef * update_coef)
    total_square = butterfly_sum(local_square, "fsdp", fsdp_radices, "fsd")
    scale_root = jnp.sqrt(total_square / (shard_rows * lax.axis_size("fsdp") * columns) + EPSILON)

    coef3 = update_coef.reshape(row_blocks, col_blocks, coef_total).transpose(0, 2, 1)
    new_params = apply_update(params, idx_t3, coef3, scale_root, OUTER_RATE)
    return (new_params, new_error, new_momentum)


def solution(mesh):
    in_specs = (
        P("island", "fsdp", None),
        P("island", "fsdp", None),
        P("fsdp", None),
        P("island", "fsdp"),
        P("island", "fsdp"),
        P("fsdp", None),
        P("fsdp"),
    )
    out_specs = (P("fsdp", None), P("island", "fsdp", None), P("island", "fsdp"))
    island_radices = radices_of((4, 12, 2))
    if mesh.shape["island"] != 96:
        island_radices = radices_of((mesh.shape["island"],))
    fsdp_radices = radices_of((mesh.shape["fsdp"],))
    body = functools.partial(on_device, island_radices, fsdp_radices)
    return jax.shard_map(
        body, mesh=mesh, in_specs=in_specs, out_specs=out_specs, check_vma=False
    )
```

```python
import functools

import jax
import jax.numpy as jnp
from jax import lax
from jax.sharding import PartitionSpec as P
from jax.experimental import pallas as pl
from jax.experimental.pallas import tpu as pltpu

BETA_FACTOR = 0.9
OUTER_RATE = 0.5
EPSILON = 1e-06
precise_mode = lax.Precision.HIGHEST


def cosine_table():
    freqs = jnp.arange(64, dtype=jnp.float32)[:, None]
    points = jnp.arange(64, dtype=jnp.float32)[None, :]
    scaling = jnp.where(freqs == 0.0, jnp.sqrt(1.0 / 64.0), jnp.sqrt(2.0 / 64.0))
    return scaling * jnp.cos(jnp.pi * (2.0 * points + 1.0) * freqs / 128.0)


def to_blocks(field):
    row_blocks = field.shape[0] // 64
    col_blocks = field.shape[1] // 64
    return (
        field.reshape(row_blocks, 64, col_blocks, 64)
        .transpose(0, 2, 1, 3)
        .reshape(row_blocks * col_blocks, 64, 64)
    )


def from_blocks(blocks, row_total, col_total):
    row_blocks = row_total // 64
    col_blocks = col_total // 64
    return (
        blocks.reshape(row_blocks, col_blocks, 64, 64)
        .transpose(0, 2, 1, 3)
        .reshape(row_total, col_total)
    )


def one_hot_rows(table, index):
    hot = (index[..., None] == jnp.arange(table.shape[0], dtype=jnp.int32)).astype(jnp.float32)
    return jnp.einsum("...t,tc->...c", hot, table, precision=precise_mode)


def decode(row_cos, col_cos, values):
    return jnp.einsum("bkj,bkl->bjl", row_cos * values[:, :, None], col_cos, precision=precise_mode)


def butterfly_sum(value, axis, radices, tag):
    size = lax.axis_size(axis)
    here = lax.axis_index(axis)
    stride = 1
    done_rounds = []
    for radix in radices:
        digit = (here // stride) % radix
        pieces = {0: value}
        for shift in range(1, radix):
            perm = []
            for src in range(size):
                d = (src // stride) % radix
                perm.append((src, src + ((d + shift) % radix - d) * stride))
            with jax.named_scope(f"{tag}{len(done_rounds)}s{shift}"):
                pieces[shift] = lax.ppermute(value, axis, perm)
        if radix == 2:
            value = pieces[0] + pieces[1]
        else:
            ordered = []
            for e in range(radix):
                pick = pieces[0]
                for shift in range(1, radix):
                    pick = jnp.where((digit - shift) % radix == e, pieces[shift], pick)
                ordered.append(pick)
            value = ordered[0]
            for e in range(1, radix):
                value = value + ordered[e]
        stride *= radix
        done_rounds.append(radix)
    return value


def radices_of(sub_sizes):
    out = []
    for part in reversed(sub_sizes):
        left = part
        for prime in (2, 3, 5, 7):
            while left % prime == 0:
                out.append(prime)
                left //= prime
        if left > 1:
            out.append(left)
    return out


def _slab_tables(idx, cos, tile):
    count = idx.shape[0]
    lanes = lax.broadcasted_iota(jnp.int32, (count, 64), 1)
    row_hot = (idx // 64 == lanes).astype(jnp.float32)
    col_hot = (idx % 64 == lanes).astype(jnp.float32)
    row_cos = jnp.dot(row_hot, cos, precision=precise_mode, preferred_element_type=jnp.float32)
    col_cos = jnp.dot(col_hot, cos, precision=precise_mode, preferred_element_type=jnp.float32)
    spread = jnp.dot(col_cos, tile, precision=precise_mode, preferred_element_type=jnp.float32)
    width = tile.shape[1]
    own = (lax.broadcasted_iota(jnp.int32, (count, width), 0) // 64) == (
        lax.broadcasted_iota(jnp.int32, (count, width), 1) // 64
    )
    return row_cos, jnp.where(own, spread, 0.0)


def _encode_kernel(cos_ref, tile_ref, idx_ref, mask_ref, g_ref, e_ref, sent_ref, err_ref):
    row_cos, col_diag = _slab_tables(idx_ref[0], cos_ref[...], tile_ref[...])
    x = g_ref[...].astype(jnp.float32) + e_ref[...].astype(jnp.float32)
    half = jnp.dot(row_cos, x, precision=precise_mode, preferred_element_type=jnp.float32)
    sent = jnp.sum(half * col_diag, axis=1, keepdims=True) * mask_ref[0]
    sent_ref[0] = sent
    rebuilt = jnp.dot((row_cos * sent).T, col_diag, precision=precise_mode, preferred_element_type=jnp.float32)
    err_ref[...] = (x - rebuilt).astype(err_ref.dtype)


def _tile_of(columns):
    return jnp.tile(jnp.eye(64, dtype=jnp.float32), (1, columns // 64))


def encode(grad, error, idx_col, mask_col):
    rows, columns = grad.shape
    row_blocks = rows // 64
    count = idx_col.shape[1]
    return pl.pallas_call(
        _encode_kernel,
        grid=(row_blocks,),
        in_specs=[
            pl.BlockSpec((64, 64), lambda i: (0, 0)),
            pl.BlockSpec((64, columns), lambda i: (0, 0)),
            pl.BlockSpec((1, count, 1), lambda i: (i, 0, 0)),
            pl.BlockSpec((1, count, 1), lambda i: (i, 0, 0)),
            pl.BlockSpec((64, columns), lambda i: (i, 0)),
            pl.BlockSpec((64, columns), lambda i: (i, 0)),
        ],
        out_specs=[
            pl.BlockSpec((1, count, 1), lambda i: (i, 0, 0)),
            pl.BlockSpec((64, columns), lambda i: (i, 0)),
        ],
        out_shape=[
            jax.ShapeDtypeStruct((row_blocks, count, 1), jnp.float32),
            jax.ShapeDtypeStruct((rows, columns), jnp.bfloat16),
        ],
        compiler_params=pltpu.CompilerParams(dimension_semantics=("parallel",)),
    )(cosine_table(), _tile_of(columns), idx_col, mask_col, grad, error)


def _apply_kernel(rate, cos_ref, tile_ref, idx_ref, coef_ref, scale_ref, p_ref, out_ref):
    row_cos, col_diag = _slab_tables(idx_ref[0], cos_ref[...], tile_ref[...])
    update = jnp.dot((row_cos * coef_ref[0]).T, col_diag, precision=precise_mode, preferred_element_type=jnp.float32)
    update = update.astype(jnp.bfloat16).astype(jnp.float32)
    out_ref[...] = (p_ref[...].astype(jnp.float32) - rate * update / scale_ref[0, 0]).astype(out_ref.dtype)


def apply_update(params, idx_col, coef_col, scale, rate):
    rows, columns = params.shape
    row_blocks = rows // 64
    count = idx_col.shape[1]
    return pl.pallas_call(
        functools.partial(_apply_kernel, rate),
        grid=(row_blocks,),
        in_specs=[
            pl.BlockSpec((64, 64), lambda i: (0, 0)),
            pl.BlockSpec((64, columns), lambda i: (0, 0)),
            pl.BlockSpec((1, count, 1), lambda i: (i, 0, 0)),
            pl.BlockSpec((1, count, 1), lambda i: (i, 0, 0)),
            pl.BlockSpec(memory_space=pltpu.SMEM),
            pl.BlockSpec((64, columns), lambda i: (i, 0)),
        ],
        out_specs=pl.BlockSpec((64, columns), lambda i: (i, 0)),
        out_shape=jax.ShapeDtypeStruct((rows, columns), jnp.bfloat16),
        compiler_params=pltpu.CompilerParams(dimension_semantics=("parallel",)),
    )(cosine_table(), _tile_of(columns), idx_col, coef_col, scale.reshape(1, 1), params)


def on_device(island_radices, fsdp_radices, pseudo_grad, error_buf, params, momentum, sel_blocks, coef_index, owner_map):
    my_island = lax.axis_index("island")
    shard_rows = params.shape[0]
    columns = params.shape[1]
    n_blocks = coef_index.shape[0]
    coef_total = coef_index.shape[1]
    capacity = momentum.shape[1] // coef_total
    row_blocks = shard_rows // 64
    col_blocks = columns // 64

    chosen = sel_blocks[0]
    block_ids = jnp.arange(n_blocks, dtype=jnp.int32)
    chosen_mask = jnp.any(chosen[:, None] == block_ids[None, :], axis=0).astype(jnp.float32)
    slab = col_blocks * coef_total
    idx_col = coef_index.reshape(row_blocks, slab, 1)
    mask_col = jnp.repeat(chosen_mask, coef_total).reshape(row_blocks, slab, 1)
    sent_col, fresh_error = encode(pseudo_grad[0], error_buf[0], idx_col, mask_col)
    new_error = fresh_error[None]
    outgoing = sent_col.reshape(n_blocks, coef_total)

    earlier = (owner_map[None, :] == owner_map[:, None]) & (block_ids[None, :] < block_ids[:, None])
    slot_of = jnp.sum(earlier.astype(jnp.int32), axis=1)
    target = owner_map * capacity + slot_of
    own_slots = my_island * capacity + jnp.arange(capacity, dtype=jnp.int32)
    owned_mask = (target[None, :] == own_slots[:, None]).astype(jnp.float32)
    mine = momentum[0].reshape(capacity, coef_total)
    held = jnp.einsum("sb,sk->bk", owned_mask, mine, precision=precise_mode)

    mask_rows = -(-n_blocks // coef_total)
    mask_part = jnp.pad(chosen_mask, (0, mask_rows * coef_total - n_blocks)).reshape(mask_rows, coef_total)
    payload = jnp.concatenate([outgoing, held, mask_part], axis=0)
    reduced = butterfly_sum(payload, "island", island_radices, "isl")
    totals = reduced[:n_blocks]
    previous = reduced[n_blocks : 2 * n_blocks]
    counts = reduced[2 * n_blocks :].reshape(-1)[:n_blocks]

    average = totals / jnp.maximum(counts, 1.0)[:, None]
    refreshed = BETA_FACTOR * previous + average
    update_coef = average + BETA_FACTOR * refreshed

    owned_live = jnp.sum(owned_mask, axis=1) > 0.0
    owned_fresh = jnp.dot(owned_mask, refreshed, precision=precise_mode)
    kept = BETA_FACTOR * mine
    new_momentum = jnp.where(owned_live[:, None], owned_fresh, kept).reshape(1, capacity * coef_total)

    local_square = jnp.sum(update_coef * update_coef)
    total_square = butterfly_sum(local_square, "fsdp", fsdp_radices, "fsd")
    scale_root = jnp.sqrt(total_square / (shard_rows * lax.axis_size("fsdp") * columns) + EPSILON)

    coef_col = update_coef.reshape(row_blocks, slab, 1)
    new_params = apply_update(params, idx_col, coef_col, scale_root, OUTER_RATE)
    return (new_params, new_error, new_momentum)


def solution(mesh):
    in_specs = (
        P("island", "fsdp", None),
        P("island", "fsdp", None),
        P("fsdp", None),
        P("island", "fsdp"),
        P("island", "fsdp"),
        P("fsdp", None),
        P("fsdp"),
    )
    out_specs = (P("fsdp", None), P("island", "fsdp", None), P("island", "fsdp"))
    island_radices = radices_of((4, 12, 2))
    if mesh.shape["island"] != 96:
        island_radices = radices_of((mesh.shape["island"],))
    fsdp_radices = radices_of((mesh.shape["fsdp"],))
    body = functools.partial(on_device, island_radices, fsdp_radices)
    return jax.shard_map(
        body, mesh=mesh, in_specs=in_specs, out_specs=out_specs, check_vma=False
    )
```

```python
import functools

import jax
import jax.numpy as jnp
from jax import lax
from jax.sharding import PartitionSpec as P

BETA_FACTOR = 0.9
OUTER_RATE = 0.5
EPSILON = 1e-06
precise_mode = lax.Precision.HIGHEST


def cosine_table():
    freqs = jnp.arange(64, dtype=jnp.float32)[:, None]
    points = jnp.arange(64, dtype=jnp.float32)[None, :]
    scaling = jnp.where(freqs == 0.0, jnp.sqrt(1.0 / 64.0), jnp.sqrt(2.0 / 64.0))
    return scaling * jnp.cos(jnp.pi * (2.0 * points + 1.0) * freqs / 128.0)


def to_blocks(field):
    row_blocks = field.shape[0] // 64
    col_blocks = field.shape[1] // 64
    return (
        field.reshape(row_blocks, 64, col_blocks, 64)
        .transpose(0, 2, 1, 3)
        .reshape(row_blocks * col_blocks, 64, 64)
    )


def from_blocks(blocks, row_total, col_total):
    row_blocks = row_total // 64
    col_blocks = col_total // 64
    return (
        blocks.reshape(row_blocks, col_blocks, 64, 64)
        .transpose(0, 2, 1, 3)
        .reshape(row_total, col_total)
    )


def one_hot_rows(table, index):
    hot = (index[..., None] == jnp.arange(table.shape[0], dtype=jnp.int32)).astype(jnp.float32)
    return jnp.einsum("...t,tc->...c", hot, table, precision=precise_mode)


def decode(row_cos, col_cos, values):
    return jnp.einsum("bkj,bkl->bjl", row_cos * values[:, :, None], col_cos, precision=precise_mode)


def butterfly_sum(value, axis, radices):
    size = lax.axis_size(axis)
    here = lax.axis_index(axis)
    stride = 1
    for radix in radices:
        digit = (here // stride) % radix
        pieces = {0: value}
        for shift in range(1, radix):
            perm = []
            for src in range(size):
                d = (src // stride) % radix
                perm.append((src, src + ((d + shift) % radix - d) * stride))
            pieces[shift] = lax.ppermute(value, axis, perm)
        if radix == 2:
            value = pieces[0] + pieces[1]
        else:
            ordered = []
            for e in range(radix):
                pick = pieces[0]
                for shift in range(1, radix):
                    pick = jnp.where((digit - shift) % radix == e, pieces[shift], pick)
                ordered.append(pick)
            value = ordered[0]
            for e in range(1, radix):
                value = value + ordered[e]
        stride *= radix
    return value


def radices_of(sub_sizes):
    out = []
    for part in reversed(sub_sizes):
        left = part
        for prime in (2, 3, 5, 7):
            while left % prime == 0:
                out.append(prime)
                left //= prime
        if left > 1:
            out.append(left)
    return out


def on_device(island_radices, fsdp_radices, pseudo_grad, error_buf, params, momentum, sel_blocks, coef_index, owner_map):
    cosine = cosine_table()
    my_island = lax.axis_index("island")
    shard_rows = params.shape[0]
    columns = params.shape[1]
    n_blocks = coef_index.shape[0]
    coef_total = coef_index.shape[1]
    capacity = momentum.shape[1] // coef_total

    summed = pseudo_grad[0].astype(jnp.float32) + error_buf[0].astype(jnp.float32)
    blocks = to_blocks(summed)
    row_cos = one_hot_rows(cosine, coef_index // 64)
    col_cos = one_hot_rows(cosine, coef_index % 64)
    half = jnp.einsum("bkj,bjl->bkl", row_cos, blocks, precision=precise_mode)
    picked = jnp.sum(half * col_cos, axis=2)

    chosen = sel_blocks[0]
    block_ids = jnp.arange(n_blocks, dtype=jnp.int32)
    chosen_mask = jnp.any(chosen[:, None] == block_ids[None, :], axis=0).astype(jnp.float32)
    outgoing = picked * chosen_mask[:, None]

    earlier = (owner_map[None, :] == owner_map[:, None]) & (block_ids[None, :] < block_ids[:, None])
    slot_of = jnp.sum(earlier.astype(jnp.int32), axis=1)
    target = owner_map * capacity + slot_of
    own_slots = my_island * capacity + jnp.arange(capacity, dtype=jnp.int32)
    owned_mask = (target[None, :] == own_slots[:, None]).astype(jnp.float32)
    mine = momentum[0].reshape(capacity, coef_total)
    held = jnp.einsum("sb,sk->bk", owned_mask, mine, precision=precise_mode)

    mask_rows = -(-n_blocks // coef_total)
    mask_part = jnp.pad(chosen_mask, (0, mask_rows * coef_total - n_blocks)).reshape(mask_rows, coef_total)
    payload = jnp.concatenate([outgoing, held, mask_part], axis=0)
    reduced = butterfly_sum(payload, "island", island_radices)
    totals = reduced[:n_blocks]
    previous = reduced[n_blocks : 2 * n_blocks]
    counts = reduced[2 * n_blocks :].reshape(-1)[:n_blocks]

    rebuilt = decode(row_cos, col_cos, outgoing)
    new_error = from_blocks(blocks - rebuilt, shard_rows, columns).astype(jnp.bfloat16)[None]

    average = totals / jnp.maximum(counts, 1.0)[:, None]
    refreshed = BETA_FACTOR * previous + average
    update_coef = average + BETA_FACTOR * refreshed

    owned_live = jnp.sum(owned_mask, axis=1) > 0.0
    owned_fresh = jnp.dot(owned_mask, refreshed, precision=precise_mode)
    kept = BETA_FACTOR * mine
    new_momentum = jnp.where(owned_live[:, None], owned_fresh, kept).reshape(1, capacity * coef_total)

    update = decode(row_cos, col_cos, update_coef).astype(jnp.bfloat16).astype(jnp.float32)
    local_square = jnp.sum(update * update)
    total_square = butterfly_sum(local_square, "fsdp", fsdp_radices)
    scale_root = jnp.sqrt(total_square / (shard_rows * lax.axis_size("fsdp") * columns) + EPSILON)
    shifted = from_blocks(update, shard_rows, columns)
    new_params = (params.astype(jnp.float32) - OUTER_RATE * shifted / scale_root).astype(
        jnp.bfloat16
    )
    return (new_params, new_error, new_momentum)


def solution(mesh):
    in_specs = (
        P("island", "fsdp", None),
        P("island", "fsdp", None),
        P("fsdp", None),
        P("island", "fsdp"),
        P("island", "fsdp"),
        P("fsdp", None),
        P("fsdp"),
    )
    out_specs = (P("fsdp", None), P("island", "fsdp", None), P("island", "fsdp"))
    island_radices = radices_of((mesh.shape["island"],))
    if mesh.shape["island"] == 96:
        island_radices = [2, 4, 3, 4]
    fsdp_radices = radices_of((mesh.shape["fsdp"],))
    if mesh.shape["fsdp"] == 8:
        fsdp_radices = [2, 4]
    body = functools.partial(on_device, island_radices, fsdp_radices)
    return jax.shard_map(
        body, mesh=mesh, in_specs=in_specs, out_specs=out_specs, check_vma=False
    )
```

```python
import functools

import jax
import jax.numpy as jnp
from jax import lax
from jax.sharding import PartitionSpec as P

BETA_FACTOR = 0.9
OUTER_RATE = 0.5
EPSILON = 1e-06
precise_mode = lax.Precision.HIGHEST


def cosine_table():
    freqs = jnp.arange(64, dtype=jnp.float32)[:, None]
    points = jnp.arange(64, dtype=jnp.float32)[None, :]
    scaling = jnp.where(freqs == 0.0, jnp.sqrt(1.0 / 64.0), jnp.sqrt(2.0 / 64.0))
    return scaling * jnp.cos(jnp.pi * (2.0 * points + 1.0) * freqs / 128.0)


def to_blocks(field):
    row_blocks = field.shape[0] // 64
    col_blocks = field.shape[1] // 64
    return (
        field.reshape(row_blocks, 64, col_blocks, 64)
        .transpose(0, 2, 1, 3)
        .reshape(row_blocks * col_blocks, 64, 64)
    )


def from_blocks(blocks, row_total, col_total):
    row_blocks = row_total // 64
    col_blocks = col_total // 64
    return (
        blocks.reshape(row_blocks, col_blocks, 64, 64)
        .transpose(0, 2, 1, 3)
        .reshape(row_total, col_total)
    )


def one_hot_rows(table, index):
    hot = (index[..., None] == jnp.arange(table.shape[0], dtype=jnp.int32)).astype(jnp.float32)
    return jnp.einsum("...t,tc->...c", hot, table, precision=precise_mode)


def butterfly_sum(value, axis, radices):
    size = lax.axis_size(axis)
    here = lax.axis_index(axis)
    stride = 1
    for radix in radices:
        digit = (here // stride) % radix
        pieces = {0: value}
        for shift in range(1, radix):
            perm = []
            for src in range(size):
                d = (src // stride) % radix
                perm.append((src, src + ((d + shift) % radix - d) * stride))
            pieces[shift] = lax.ppermute(value, axis, perm)
        if radix == 2:
            value = pieces[0] + pieces[1]
        else:
            ordered = []
            for e in range(radix):
                pick = pieces[0]
                for shift in range(1, radix):
                    pick = jnp.where((digit - shift) % radix == e, pieces[shift], pick)
                ordered.append(pick)
            value = ordered[0]
            for e in range(1, radix):
                value = value + ordered[e]
        stride *= radix
    return value


def radices_of(sub_sizes):
    out = []
    for part in reversed(sub_sizes):
        left = part
        for prime in (2, 3, 5, 7):
            while left % prime == 0:
                out.append(prime)
                left //= prime
        if left > 1:
            out.append(left)
    return out


def on_device(island_radices, fsdp_radices, *args):
    return step_body(island_radices, fsdp_radices, *args)


def step_body(island_radices, fsdp_radices, pseudo_grad, error_buf, params, momentum, sel_blocks, coef_index, owner_map):
    cosine = cosine_table()
    my_island = lax.axis_index("island")
    shard_rows = params.shape[0]
    columns = params.shape[1]
    n_blocks = coef_index.shape[0]
    coef_total = coef_index.shape[1]
    capacity = momentum.shape[1] // coef_total

    summed = pseudo_grad[0].astype(jnp.float32) + error_buf[0].astype(jnp.float32)
    blocks = to_blocks(summed)
    row_cos = one_hot_rows(cosine, coef_index // 64)
    col_cos = one_hot_rows(cosine, coef_index % 64)
    half = jnp.einsum("bkj,bjl->bkl", row_cos, blocks, precision=precise_mode)
    picked = jnp.sum(half * col_cos, axis=2)

    chosen = sel_blocks[0]
    block_ids = jnp.arange(n_blocks, dtype=jnp.int32)
    chosen_mask = jnp.any(chosen[:, None] == block_ids[None, :], axis=0).astype(jnp.float32)
    outgoing = picked * chosen_mask[:, None]

    earlier = (owner_map[None, :] == owner_map[:, None]) & (block_ids[None, :] < block_ids[:, None])
    slot_of = jnp.sum(earlier.astype(jnp.int32), axis=1)
    target = owner_map * capacity + slot_of
    own_slots = my_island * capacity + jnp.arange(capacity, dtype=jnp.int32)
    owned_mask = (target[None, :] == own_slots[:, None]).astype(jnp.float32)
    mine = momentum[0].reshape(capacity, coef_total)
    held = jnp.einsum("sb,sk->bk", owned_mask, mine, precision=precise_mode)

    mask_rows = -(-n_blocks // coef_total)
    mask_part = jnp.pad(chosen_mask, (0, mask_rows * coef_total - n_blocks)).reshape(mask_rows, coef_total)
    payload = jnp.concatenate([outgoing, held, mask_part], axis=0)
    reduced = butterfly_sum(payload, "island", island_radices)
    totals = reduced[:n_blocks]
    previous = reduced[n_blocks : 2 * n_blocks]
    counts = reduced[2 * n_blocks :].reshape(-1)[:n_blocks]

    err_rows, err_cols, err_sent = lax.optimization_barrier((row_cos, col_cos, outgoing))
    scaled = err_rows * err_sent[:, :, None]
    fresh = blocks - jnp.einsum("bkj,bkl->bjl", scaled, err_cols, precision=precise_mode)
    new_error = from_blocks(fresh, shard_rows, columns).astype(jnp.bfloat16)[None]

    average = totals / jnp.maximum(counts, 1.0)[:, None]
    refreshed = BETA_FACTOR * previous + average
    update_coef = average + BETA_FACTOR * refreshed

    owned_live = jnp.sum(owned_mask, axis=1) > 0.0
    owned_fresh = jnp.dot(owned_mask, refreshed, precision=precise_mode)
    kept = BETA_FACTOR * mine
    new_momentum = jnp.where(owned_live[:, None], owned_fresh, kept).reshape(1, capacity * coef_total)

    local_square = jnp.sum(update_coef * update_coef)
    total_square = butterfly_sum(local_square, "fsdp", fsdp_radices)
    scale_root = jnp.sqrt(total_square / (shard_rows * lax.axis_size("fsdp") * columns) + EPSILON)
    scaled_update = row_cos * update_coef[:, :, None]
    update = jnp.einsum("bkj,bkl->bjl", scaled_update, col_cos, precision=precise_mode)
    update = lax.optimization_barrier(update.astype(jnp.bfloat16))
    shifted = from_blocks(update, shard_rows, columns).astype(jnp.float32)
    new_params = (params.astype(jnp.float32) - OUTER_RATE * shifted / scale_root).astype(
        jnp.bfloat16
    )
    return (new_params, new_error, new_momentum)


def solution(mesh):
    in_specs = (
        P("island", "fsdp", None),
        P("island", "fsdp", None),
        P("fsdp", None),
        P("island", "fsdp"),
        P("island", "fsdp"),
        P("fsdp", None),
        P("fsdp"),
    )
    out_specs = (P("fsdp", None), P("island", "fsdp", None), P("island", "fsdp"))
    island_radices = radices_of((4, 12, 2))
    if mesh.shape["island"] != 96:
        island_radices = radices_of((mesh.shape["island"],))
    fsdp_radices = radices_of((mesh.shape["fsdp"],))
    body = functools.partial(on_device, island_radices, fsdp_radices)
    return jax.shard_map(
        body, mesh=mesh, in_specs=in_specs, out_specs=out_specs, check_vma=False
    )
```

```python
import functools

import jax
import jax.numpy as jnp
from jax import lax
from jax.sharding import PartitionSpec as P

BETA_FACTOR = 0.9
OUTER_RATE = 0.5
EPSILON = 1e-06
precise_mode = lax.Precision.HIGHEST


def cosine_table():
    freqs = jnp.arange(64, dtype=jnp.float32)[:, None]
    points = jnp.arange(64, dtype=jnp.float32)[None, :]
    scaling = jnp.where(freqs == 0.0, jnp.sqrt(1.0 / 64.0), jnp.sqrt(2.0 / 64.0))
    return scaling * jnp.cos(jnp.pi * (2.0 * points + 1.0) * freqs / 128.0)


def to_blocks(field):
    row_blocks = field.shape[0] // 64
    col_blocks = field.shape[1] // 64
    return (
        field.reshape(row_blocks, 64, col_blocks, 64)
        .transpose(0, 2, 1, 3)
        .reshape(row_blocks * col_blocks, 64, 64)
    )


def from_blocks(blocks, row_total, col_total):
    row_blocks = row_total // 64
    col_blocks = col_total // 64
    return (
        blocks.reshape(row_blocks, col_blocks, 64, 64)
        .transpose(0, 2, 1, 3)
        .reshape(row_total, col_total)
    )


def one_hot_rows(table, index):
    return jnp.take(table, index, axis=0)


def decode(row_cos, col_cos, values):
    return jnp.einsum("bkj,bkl->bjl", row_cos * values[:, :, None], col_cos, precision=precise_mode)


def butterfly_sum(value, axis, radices):
    size = lax.axis_size(axis)
    here = lax.axis_index(axis)
    stride = 1
    for radix in radices:
        digit = (here // stride) % radix
        pieces = {0: value}
        for shift in range(1, radix):
            perm = []
            for src in range(size):
                d = (src // stride) % radix
                perm.append((src, src + ((d + shift) % radix - d) * stride))
            pieces[shift] = lax.ppermute(value, axis, perm)
        if radix == 2:
            value = pieces[0] + pieces[1]
        else:
            ordered = []
            for e in range(radix):
                pick = pieces[0]
                for shift in range(1, radix):
                    pick = jnp.where((digit - shift) % radix == e, pieces[shift], pick)
                ordered.append(pick)
            value = ordered[0]
            for e in range(1, radix):
                value = value + ordered[e]
        stride *= radix
    return value


def radices_of(sub_sizes):
    out = []
    for part in reversed(sub_sizes):
        left = part
        for prime in (2, 3, 5, 7):
            while left % prime == 0:
                out.append(prime)
                left //= prime
        if left > 1:
            out.append(left)
    return out


def on_device(island_radices, fsdp_radices, *args):
    return step_body(island_radices, fsdp_radices, *args)


def step_body(island_radices, fsdp_radices, pseudo_grad, error_buf, params, momentum, sel_blocks, coef_index, owner_map):
    cosine = cosine_table()
    my_island = lax.axis_index("island")
    shard_rows = params.shape[0]
    columns = params.shape[1]
    n_blocks = coef_index.shape[0]
    coef_total = coef_index.shape[1]
    capacity = momentum.shape[1] // coef_total

    summed = pseudo_grad[0].astype(jnp.float32) + error_buf[0].astype(jnp.float32)
    blocks = to_blocks(summed)
    row_cos = one_hot_rows(cosine, coef_index // 64)
    col_cos = one_hot_rows(cosine, coef_index % 64)
    half = jnp.einsum("bkj,bjl->bkl", row_cos, blocks, precision=precise_mode)
    picked = jnp.sum(half * col_cos, axis=2)

    chosen = sel_blocks[0]
    block_ids = jnp.arange(n_blocks, dtype=jnp.int32)
    chosen_mask = jnp.any(chosen[:, None] == block_ids[None, :], axis=0).astype(jnp.float32)
    outgoing = picked * chosen_mask[:, None]

    earlier = (owner_map[None, :] == owner_map[:, None]) & (block_ids[None, :] < block_ids[:, None])
    slot_of = jnp.sum(earlier.astype(jnp.int32), axis=1)
    target = owner_map * capacity + slot_of
    own_slots = my_island * capacity + jnp.arange(capacity, dtype=jnp.int32)
    owned_mask = (target[None, :] == own_slots[:, None]).astype(jnp.float32)
    mine = momentum[0].reshape(capacity, coef_total)
    held = jnp.einsum("sb,sk->bk", owned_mask, mine, precision=precise_mode)

    mask_rows = -(-n_blocks // coef_total)
    mask_part = jnp.pad(chosen_mask, (0, mask_rows * coef_total - n_blocks)).reshape(mask_rows, coef_total)
    payload = jnp.concatenate([outgoing, held, mask_part], axis=0)
    reduced = butterfly_sum(payload, "island", island_radices)
    totals = reduced[:n_blocks]
    previous = reduced[n_blocks : 2 * n_blocks]
    counts = reduced[2 * n_blocks :].reshape(-1)[:n_blocks]

    err_rows, err_cols, err_sent = lax.optimization_barrier((row_cos, col_cos, outgoing))
    scaled = err_rows * err_sent[:, :, None]
    fresh = blocks - jnp.einsum("bkj,bkl->bjl", scaled, err_cols, precision=precise_mode)
    new_error = from_blocks(fresh, shard_rows, columns).astype(jnp.bfloat16)[None]

    average = totals / jnp.maximum(counts, 1.0)[:, None]
    refreshed = BETA_FACTOR * previous + average
    update_coef = average + BETA_FACTOR * refreshed

    owned_live = jnp.sum(owned_mask, axis=1) > 0.0
    owned_fresh = jnp.dot(owned_mask, refreshed, precision=precise_mode)
    kept = BETA_FACTOR * mine
    new_momentum = jnp.where(owned_live[:, None], owned_fresh, kept).reshape(1, capacity * coef_total)

    update = decode(row_cos, col_cos, update_coef).astype(jnp.bfloat16).astype(jnp.float32)
    local_square = jnp.sum(update * update)
    total_square = butterfly_sum(local_square, "fsdp", fsdp_radices)
    scale_root = jnp.sqrt(total_square / (shard_rows * lax.axis_size("fsdp") * columns) + EPSILON)
    shifted = from_blocks(update, shard_rows, columns)
    new_params = (params.astype(jnp.float32) - OUTER_RATE * shifted / scale_root).astype(
        jnp.bfloat16
    )
    return (new_params, new_error, new_momentum)


def solution(mesh):
    in_specs = (
        P("island", "fsdp", None),
        P("island", "fsdp", None),
        P("fsdp", None),
        P("island", "fsdp"),
        P("island", "fsdp"),
        P("fsdp", None),
        P("fsdp"),
    )
    out_specs = (P("fsdp", None), P("island", "fsdp", None), P("island", "fsdp"))
    island_radices = radices_of((4, 12, 2))
    if mesh.shape["island"] != 96:
        island_radices = radices_of((mesh.shape["island"],))
    fsdp_radices = radices_of((mesh.shape["fsdp"],))
    body = functools.partial(on_device, island_radices, fsdp_radices)
    return jax.shard_map(
        body, mesh=mesh, in_specs=in_specs, out_specs=out_specs, check_vma=False
    )
```
